128 devices in a mesh: pts: 32 (over y, z, core), heads: 4 (over x).
Axes of the slice: x: 4, y: 4, z: 4, core: 2. Of those that a mesh axis runs over, the one named last changes fastest.
Arguments:
- points: bfloat16 [65536, 512], P('pts'), may hold values from -30 to 30
- perm: int32 [2, 512], replicated, may hold values from 0 to 511, as said below
- counts: int32 [2, 64], replicated, may hold values from 128 to 1024, as said below
- ln_attn: float32 [2, 512], replicated, may hold values from 0.1 to 1.9
- w_query: bfloat16 [2, 512, 512], P(None, None, 'heads'), may hold values from -48 to 48
- w_key: bfloat16 [2, 512, 512], P(None, None, 'heads'), may hold values from -1 to 1
- w_value: bfloat16 [2, 512, 512], P(None, None, 'heads'), may hold values from -0.25 to 0.25
- w_proj: bfloat16 [2, 512, 512], replicated, may hold values from -0.25 to 0.25
- ln_mlp: float32 [2, 512], replicated, may hold values from 0.1 to 1.9
- w_up: bfloat16 [2, 512, 2048], P(None, None, 'heads'), may hold values from -0.25 to 0.25
- w_down: bfloat16 [2, 2048, 512], P(None, 'heads'), may hold values from -0.125 to 0.125
Outputs:
- encoded: bfloat16 [65536, 512], P('pts')
The draws below stay inside these ranges and needn't reach their ends.
Inputs may be any that keep to these rules, and one draw needn't show every extreme that they name: `perm`: for each layer a permutation of the 512 block numbers; of the blocks that the rows of one index of pts take, at most 1 come from the rows of any one index, and in every layer some pair of indices reaches 1. The first counts[l, p] positions of patch p of layer l are live.
All inputs are finite; a program needn't handle non-finite values.
Results may differ from the reference program's by a relative error of at most 0.038.
The reference program's roundings to bfloat16 on the way (of `grouped`, `normed`, `values`, `weights`, `heads_out`, `residual`, `normed_mlp` and `hidden`) count: a program that leaves them out, or rounds other values in their place, can miss the bound.
Values may be sent and summed in bfloat16 or wider, within the bound.
No kernel may reach another device: no remote copies, remote signals or barrier semaphores. Data moves between devices by JAX's collectives and lax.ppermute only.
A program may use at most 64 MiB of HBM per device.

```python
import math
import jax
import jax.numpy as jnp
from jax import lax

C = 512
HEADS = 32
FF = 2048
PATCH = 1024
BLOCK = 128
LAYERS = 2
HD = 16
HALF = 512
NB_DEV = 16
SHARDS = 32
FF_GROUPS = 4
PATCHES = 64
ROWS = 65536
NBLK = 512


def draw_points(key, part):
    first_key, second_key, third_key = jax.random.split(key, 3)
    samples = jnp.clip(jax.random.normal(first_key, (ROWS, C), jnp.float32), -6.0, 6.0)
    log_low = math.log(0.5)
    log_high = math.log(2.0)
    row_scale = jnp.exp(jax.random.uniform(second_key, (ROWS, 1), jnp.float32, log_low, log_high))
    col_scale = jnp.exp(jax.random.uniform(third_key, (1, C), jnp.float32, log_low, log_high))
    return (samples * row_scale * col_scale).astype(jnp.bfloat16)


def key_matrix(key):
    base_key = jax.random.fold_in(key, 7)
    samples = jnp.clip(jax.random.normal(base_key, (LAYERS, C, C), jnp.float32), -6.0, 6.0)
    return samples * (1.0 / math.sqrt(C))


def draw_w_key(key, part):
    return key_matrix(key).astype(jnp.bfloat16)


def draw_w_query(key, part):
    own_key = jax.random.fold_in(key, 11)
    samples = jnp.clip(jax.random.normal(own_key, (LAYERS, C, C), jnp.float32), -6.0, 6.0)
    return (samples * (1.0 / math.sqrt(C))).astype(jnp.bfloat16)


def shuffled(subkey):
    return jax.random.permutation(subkey, NB_DEV).astype(jnp.int32)


def draw_perm(key, part):
    tables = []
    for layer_index in range(LAYERS):
        layer_key = jax.random.fold_in(key, 100 + layer_index)
        key_list = jax.random.split(layer_key, 5)
        offsets = jax.random.permutation(key_list[0], SHARDS).astype(jnp.int32)
        source_label = jax.random.permutation(key_list[1], SHARDS).astype(jnp.int32)
        target_label = jax.random.permutation(key_list[2], SHARDS).astype(jnp.int32)
        shard_ids = jnp.arange(SHARDS, dtype=jnp.int32)
        source_inverse = jnp.zeros(SHARDS, jnp.int32).at[source_label].set(shard_ids)
        target_inverse = jnp.zeros(SHARDS, jnp.int32).at[target_label].set(shard_ids)
        target_ids = shard_ids[:, None]
        slot_ids = jnp.arange(NB_DEV, dtype=jnp.int32)[None, :]
        source_shard = source_inverse[(target_inverse[target_ids] - offsets[slot_ids % SHARDS]) % SHARDS]
        local_orders = jax.vmap(shuffled)(jax.random.split(key_list[3], SHARDS))
        source_block = local_orders[source_shard, jnp.broadcast_to(slot_ids, source_shard.shape)]
        placement = jax.vmap(shuffled)(jax.random.split(key_list[4], SHARDS))
        targets = target_ids * NB_DEV + placement
        sources = source_shard * NB_DEV + source_block
        table = jnp.zeros(NBLK, jnp.int32).at[targets.reshape(-1)].set(sources.reshape(-1).astype(jnp.int32))
        tables.append(table)
    return jnp.stack(tables)


def draw_counts(key, part):
    first_key, second_key, third_key, fourth_key = jax.random.split(key, 4)
    levels = jax.random.randint(first_key, (LAYERS, PATCHES), 1, 9)
    extra = jax.random.randint(second_key, (LAYERS, PATCHES), 0, PATCH // 8)
    live = jnp.minimum(PATCH, PATCH // 8 * levels + extra)
    fullest = jax.random.randint(third_key, (LAYERS, 1), 0, PATCHES)
    emptiest = (fullest + 1 + jax.random.randint(fourth_key, (LAYERS, 1), 0, PATCHES - 1)) % PATCHES
    positions = jnp.arange(PATCHES, dtype=jnp.int32)[None, :]
    live = jnp.where(positions == fullest, PATCH, jnp.where(positions == emptiest, PATCH // 8, live))
    return live.astype(jnp.int32)


def steps_of(stream_key, dims, shards, low, top_value):
    factor_of = 1.0
    for dim, shards_of in shards:
        draws = jax.random.uniform(jax.random.fold_in(jax.random.fold_in(stream_key, 6), dim), (shards_of,), jnp.float32, low / len(shards), top_value / len(shards))
        factor_of = factor_of * jnp.repeat(jnp.exp(draws), dims[dim] // shards_of).reshape((-1,) + (1,) * (len(dims) - 1 - dim))
    return factor_of


def noise(stream_key, dims, scale, most, cuts=(), kind=jnp.bfloat16):
    array = jax.random.normal(stream_key, dims, jnp.float32) * scale
    if len(cuts) > 0:
        array = steps_of(stream_key, dims, cuts, -0.22, 0.18) * array
    return jnp.clip(array, min=-most, max=most).astype(kind)


def setup_inputs(seed: int = 0) -> dict:
    key_of = jax.random.split(jax.random.key(seed), 12)
    return {
        "points": draw_points(jax.random.fold_in(key_of[11], 71), 0),
        "perm": draw_perm(jax.random.fold_in(key_of[11], 71), 0),
        "counts": draw_counts(jax.random.fold_in(key_of[11], 71), 0),
        "ln_attn": jnp.clip(1.0 + 0.18 * jax.random.normal(key_of[3], (LAYERS, C), jnp.float32), 0.1, 1.9),
        "w_query": draw_w_query(jax.random.fold_in(key_of[11], 71), 0),
        "w_key": draw_w_key(jax.random.fold_in(key_of[11], 71), 0),
        "w_value": noise(key_of[6], (LAYERS, C, C), C ** -0.5, 0.25, ((2, 4),)),
        "w_proj": noise(key_of[7], (LAYERS, C, C), C ** -0.5, 0.25),
        "ln_mlp": jnp.clip(1.0 + 0.18 * jax.random.normal(key_of[8], (LAYERS, C), jnp.float32), 0.1, 1.9),
        "w_up": noise(key_of[9], (LAYERS, C, FF), C ** -0.5, 0.25, ((2, 4),)),
        "w_down": noise(key_of[10], (LAYERS, FF, C), FF ** -0.5, 0.125, ((1, 4),)),
    }


def layer_norm(activations, gain_row):
    widened = activations.astype(jnp.float32)
    row_mean = lax.optimization_barrier(jnp.mean(widened, axis=-1, keepdims=True))
    centred = widened - row_mean
    row_var = lax.optimization_barrier(jnp.mean(centred * centred, axis=-1, keepdims=True))
    return (centred * lax.rsqrt(row_var + 1e-05) * gain_row).astype(jnp.bfloat16)

def patch_attention(queries, key_rows, values, live_counts):
    score_scale = 1.0 / math.sqrt(HD)

    def one_patch(operands):
        query_tile, key_tile, value_tile, live_count = operands
        scores = jnp.einsum('qhd,khd->hqk', query_tile.astype(jnp.float32), key_tile.astype(jnp.float32), precision=lax.Precision.HIGHEST) * score_scale
        live = jnp.arange(PATCH, dtype=jnp.int32) < live_count
        scores = jnp.where(live[None, None, :], scores, -1e+30)
        row_peak = lax.optimization_barrier(jnp.max(scores, axis=-1, keepdims=True))
        expsum = jnp.exp(scores - row_peak)
        row_total = lax.optimization_barrier(jnp.sum(expsum, axis=-1, keepdims=True))
        weights = (expsum / row_total).astype(jnp.bfloat16)
        merged = jnp.einsum('hqk,khd->qhd', weights.astype(jnp.float32), value_tile.astype(jnp.float32))
        return merged.astype(jnp.bfloat16)
    return lax.map(one_patch, (queries, key_rows, values, live_counts))

def reference(points, perm, counts, ln_attn, w_query, w_key, w_value, w_proj, ln_mlp, w_up, w_down):
    stream = points
    group_width = FF // FF_GROUPS
    for layer_index in range(LAYERS):
        grouped = stream.reshape(NBLK, BLOCK, C)[perm[layer_index]].reshape(ROWS, C)
        normed = layer_norm(grouped, ln_attn[layer_index])
        queries = jnp.dot(normed, w_query[layer_index], preferred_element_type=jnp.float32)
        key_rows = jnp.dot(normed, w_key[layer_index], preferred_element_type=jnp.float32)
        values = jnp.dot(normed, w_value[layer_index], preferred_element_type=jnp.float32).astype(jnp.bfloat16)
        offset = HALF if layer_index % 2 == 1 else 0

        def framed(matrix):
            return jnp.roll(matrix, -offset, axis=0).reshape(PATCHES, PATCH, HEADS, HD)
        heads_out = patch_attention(framed(queries), framed(key_rows), framed(values), counts[layer_index])
        heads_out = jnp.roll(heads_out.reshape(ROWS, C), offset, axis=0)
        residual = (grouped.astype(jnp.float32) + jnp.dot(heads_out, w_proj[layer_index], preferred_element_type=jnp.float32)).astype(jnp.bfloat16)
        normed_mlp = layer_norm(residual, ln_mlp[layer_index])
        hidden = jax.nn.gelu(jnp.dot(normed_mlp, w_up[layer_index], preferred_element_type=jnp.float32), approximate=False).astype(jnp.bfloat16)
        mlp_out = jnp.zeros((ROWS, C), jnp.float32)
        for group_index in range(FF_GROUPS):
            lower = group_index * group_width
            term = jnp.dot(hidden[:, lower:lower + group_width], w_down[layer_index][lower:lower + group_width], preferred_element_type=jnp.float32).astype(jnp.bfloat16)
            term = lax.optimization_barrier(term)
            mlp_out = mlp_out + term.astype(jnp.float32)
        stream = (residual.astype(jnp.float32) + mlp_out).astype(jnp.bfloat16)
    return stream
```

```python
import math

import jax
import jax.numpy as jnp
from jax import lax
from jax.sharding import PartitionSpec as P

PATCH = 1024
BLOCK = 128
LAYERS = 2
HD = 16
HALF = 512


def from_behind(block, axis, distance):
    devices = range(lax.axis_size(axis))
    route = [((i - distance) % len(devices), i) for i in devices]
    return lax.ppermute(block, axis, route)


def layer_norm(activations, gain_row):
    widened = activations.astype(jnp.float32)
    row_mean = jnp.mean(widened, axis=-1, keepdims=True)
    centred = widened - row_mean
    row_var = jnp.mean(centred * centred, axis=-1, keepdims=True)
    return (centred * lax.rsqrt(row_var + 1e-05) * gain_row).astype(jnp.bfloat16)


def split_three(matrix):
    hi = matrix.astype(jnp.bfloat16)
    rest = matrix - hi.astype(jnp.float32)
    mid = rest.astype(jnp.bfloat16)
    lo = (rest - mid.astype(jnp.float32)).astype(jnp.bfloat16)
    return hi, mid, lo


def patch_attention(queries, key_rows, values, live_counts):
    score_scale = 1.0 / math.sqrt(HD)
    local_heads = queries.shape[2]
    pair_count = local_heads // 2

    def one_patch(operands):
        query_tile, key_tile, value_tile, live_count = operands
        live = jnp.arange(PATCH, dtype=jnp.int32) < live_count
        query_pairs = jnp.moveaxis(query_tile.reshape(PATCH, pair_count, 2, HD), 1, 0)
        key_pairs = jnp.moveaxis(key_tile.reshape(PATCH, pair_count, 2, HD), 1, 0)
        value_pairs = jnp.moveaxis(value_tile.reshape(PATCH, pair_count, 2, HD), 1, 0)

        def one_pair(pair_operands):
            query_part, key_part, value_part = pair_operands
            q_hi, q_mid, q_lo = split_three(query_part * score_scale)
            k_hi, k_mid, k_lo = split_three(key_part)
            stacked_q = jnp.concatenate([q_hi, q_hi, q_mid, q_hi, q_lo, q_mid], axis=-1)
            stacked_k = jnp.concatenate([k_hi, k_mid, k_hi, k_lo, k_hi, k_mid], axis=-1)
            scores = jnp.einsum(
                "qhd,khd->hqk", stacked_q, stacked_k, preferred_element_type=jnp.float32
            )
            scores = jnp.where(live[None, None, :], scores, -1e30)
            row_peak = jnp.max(scores, axis=-1, keepdims=True)
            expsum = jnp.exp(scores - row_peak)
            row_total = jnp.sum(expsum, axis=-1, keepdims=True)
            weights = (expsum / row_total).astype(jnp.bfloat16)
            merged = jnp.einsum(
                "hqk,khd->qhd", weights, value_part, preferred_element_type=jnp.float32
            )
            return merged.astype(jnp.bfloat16)

        merged_pairs = lax.map(one_pair, (query_pairs, key_pairs, value_pairs))
        return jnp.moveaxis(merged_pairs, 0, 1).reshape(PATCH, local_heads, HD)

    return lax.map(one_patch, (queries, key_rows, values, live_counts))


def regroup(stream, block_table, my_shard):
    shard_count = lax.axis_size("pts")
    row_count, col_count = stream.shape
    block_count = row_count // BLOCK
    slot_count = -(-block_count // shard_count)
    layout_grid = block_table.reshape(shard_count, block_count)
    source_shard = layout_grid // block_count
    source_block = layout_grid % block_count
    from_mine = (source_shard == my_shard).astype(jnp.int32)
    send_rank = jnp.cumsum(from_mine, axis=1) - 1
    slot_ids = jnp.arange(slot_count, dtype=jnp.int32)
    chosen = (from_mine[:, :, None] == 1) & (send_rank[:, :, None] == slot_ids[None, None, :])
    send_block = jnp.sum(jnp.where(chosen, source_block[:, :, None], 0), axis=1)
    occupied = jnp.any(chosen, axis=1)
    blocks = stream.reshape(block_count, BLOCK, col_count)
    outgoing = blocks[send_block.reshape(-1)].reshape(shard_count, slot_count, BLOCK, col_count)
    outgoing = jnp.where(occupied[:, :, None, None], outgoing, jnp.zeros((), stream.dtype))
    incoming = lax.all_to_all(outgoing, "pts", split_axis=0, concat_axis=0, tiled=True)
    my_sources = source_shard[my_shard]
    positions = jnp.arange(block_count, dtype=jnp.int32)
    earlier = (my_sources[None, :] == my_sources[:, None]) & (
        positions[None, :] < positions[:, None]
    )
    slot_of = jnp.sum(earlier.astype(jnp.int32), axis=1)
    received_blocks = incoming.reshape(shard_count * slot_count, BLOCK, col_count)
    return received_blocks[my_sources * slot_count + slot_of].reshape(row_count, col_count)


def shards(points, perm, counts, ln_attn, w_query, w_key, w_value, w_proj, ln_mlp, w_up, w_down):
    my_shard = lax.axis_index("pts")
    row_count = points.shape[0]
    patch_count = row_count // PATCH
    stream = points
    for layer_index in range(LAYERS):
        shifted = layer_index % 2 == 1
        stream = regroup(stream, perm[layer_index], my_shard)
        if shifted:
            incoming_tile = from_behind(stream[:HALF], "pts", -1)
            stream = jnp.concatenate([stream[HALF:], incoming_tile], axis=0)
        full_rows = stream
        live_counts = lax.dynamic_slice_in_dim(
            counts[layer_index], my_shard * patch_count, patch_count
        )
        normed = layer_norm(full_rows, ln_attn[layer_index])
        queries = jnp.dot(normed, w_query[layer_index], preferred_element_type=jnp.float32)
        key_rows = jnp.dot(normed, w_key[layer_index], preferred_element_type=jnp.float32)
        values = jnp.dot(normed, w_value[layer_index], preferred_element_type=jnp.float32).astype(
            jnp.bfloat16
        )
        local_heads = queries.shape[1] // HD

        def to_tiles(matrix):
            return matrix.reshape(patch_count, PATCH, local_heads, HD)

        heads_out = patch_attention(
            to_tiles(queries), to_tiles(key_rows), to_tiles(values), live_counts
        )
        heads_out = heads_out.reshape(row_count, local_heads * HD)
        proj_weight = w_proj[layer_index]
        attn_mixed = jnp.dot(
            lax.all_gather(heads_out, "heads", axis=1, tiled=True),
            proj_weight,
            preferred_element_type=jnp.float32,
        )
        residual = (full_rows.astype(jnp.float32) + attn_mixed).astype(jnp.bfloat16)
        normed_mlp = layer_norm(residual, ln_mlp[layer_index])
        hidden = jax.nn.gelu(
            jnp.dot(normed_mlp, w_up[layer_index], preferred_element_type=jnp.float32),
            approximate=False,
        ).astype(jnp.bfloat16)
        mlp_terms = jnp.dot(hidden, w_down[layer_index], preferred_element_type=jnp.float32)
        mlp_total = lax.psum(mlp_terms.astype(jnp.bfloat16), "heads").astype(jnp.float32)
        stream = (residual.astype(jnp.float32) + mlp_total).astype(jnp.bfloat16)
        if shifted:
            outgoing_tile = from_behind(stream[row_count - HALF :], "pts", 1)
            stream = jnp.concatenate([outgoing_tile, stream[: row_count - HALF]], axis=0)
    return stream


def solution(mesh):
    placed = (
        P("pts", None),
        P(),
        P(),
        P(),
        P(None, None, "heads"),
        P(None, None, "heads"),
        P(None, None, "heads"),
        P(),
        P(),
        P(None, None, "heads"),
        P(None, "heads", None),
    )
    return jax.shard_map(
        shards, mesh=mesh, in_specs=placed, out_specs=P("pts", None), check_vma=False
    )
```

```python
import math

import jax
import jax.numpy as jnp
from jax import lax
from jax.sharding import PartitionSpec as P

PATCH = 1024
BLOCK = 128
LAYERS = 2
HD = 16
HALF = 512
FF_GROUPS = 4


def from_behind(block, axis, distance):
    devices = range(lax.axis_size(axis))
    route = [((i - distance) % len(devices), i) for i in devices]
    return lax.ppermute(block, axis, route)


def layer_norm(activations, gain_row):
    widened = activations.astype(jnp.float32)
    row_mean = jnp.mean(widened, axis=-1, keepdims=True)
    centred = widened - row_mean
    row_var = jnp.mean(centred * centred, axis=-1, keepdims=True)
    return (centred * lax.rsqrt(row_var + 1e-05) * gain_row).astype(jnp.bfloat16)


def patch_attention(queries, key_rows, values, live_counts):
    score_scale = 1.0 / math.sqrt(HD)
    local_heads = queries.shape[2]
    pair_count = local_heads // 2

    def one_patch(operands):
        query_tile, key_tile, value_tile, live_count = operands
        live = jnp.arange(PATCH, dtype=jnp.int32) < live_count
        query_pairs = jnp.moveaxis(query_tile.reshape(PATCH, pair_count, 2, HD), 1, 0)
        key_pairs = jnp.moveaxis(key_tile.reshape(PATCH, pair_count, 2, HD), 1, 0)
        value_pairs = jnp.moveaxis(value_tile.reshape(PATCH, pair_count, 2, HD), 1, 0)

        def one_pair(pair_operands):
            query_part, key_part, value_part = pair_operands
            scores = (
                jnp.einsum(
                    "qhd,khd->hqk",
                    query_part,
                    key_part,
                    precision=lax.Precision.HIGHEST,
                    preferred_element_type=jnp.float32,
                )
                * score_scale
            )
            scores = jnp.where(live[None, None, :], scores, -1e30)
            row_peak = jnp.max(scores, axis=-1, keepdims=True)
            expsum = jnp.exp(scores - row_peak)
            row_total = jnp.sum(expsum, axis=-1, keepdims=True)
            weights = (expsum / row_total).astype(jnp.bfloat16)
            merged = jnp.einsum(
                "hqk,khd->qhd", weights, value_part, preferred_element_type=jnp.float32
            )
            return merged.astype(jnp.bfloat16)

        merged_pairs = lax.map(one_pair, (query_pairs, key_pairs, value_pairs))
        return jnp.moveaxis(merged_pairs, 0, 1).reshape(PATCH, local_heads, HD)

    return lax.map(one_patch, (queries, key_rows, values, live_counts))


def regroup(pieces, block_table, my_shard):
    shard_count = lax.axis_size("pts")
    block_count, piece_rows, col_count = pieces.shape
    slot_count = -(-block_count // shard_count)
    layout_grid = block_table.reshape(shard_count, block_count)
    source_shard = layout_grid // block_count
    source_block = layout_grid % block_count
    from_mine = (source_shard == my_shard).astype(jnp.int32)
    send_rank = jnp.cumsum(from_mine, axis=1) - 1
    slot_ids = jnp.arange(slot_count, dtype=jnp.int32)
    chosen = (from_mine[:, :, None] == 1) & (send_rank[:, :, None] == slot_ids[None, None, :])
    send_block = jnp.sum(jnp.where(chosen, source_block[:, :, None], 0), axis=1)
    occupied = jnp.any(chosen, axis=1)
    outgoing = pieces[send_block.reshape(-1)].reshape(shard_count, slot_count, piece_rows, col_count)
    outgoing = jnp.where(occupied[:, :, None, None], outgoing, jnp.zeros((), pieces.dtype))
    incoming = lax.all_to_all(outgoing, "pts", split_axis=0, concat_axis=0, tiled=True)
    my_sources = source_shard[my_shard]
    positions = jnp.arange(block_count, dtype=jnp.int32)
    earlier = (my_sources[None, :] == my_sources[:, None]) & (
        positions[None, :] < positions[:, None]
    )
    slot_of = jnp.sum(earlier.astype(jnp.int32), axis=1)
    received_blocks = incoming.reshape(shard_count * slot_count, piece_rows, col_count)
    return received_blocks[my_sources * slot_count + slot_of]


def gather_rows(pieces):
    block_count, _, col_count = pieces.shape
    whole = lax.all_gather(pieces, "heads", axis=1)
    return whole.reshape(block_count * BLOCK, col_count)


def shards(points, perm, counts, ln_attn, w_query, w_key, w_value, w_proj, ln_mlp, w_up, w_down):
    my_shard = lax.axis_index("pts")
    my_quarter = lax.axis_index("heads")
    quarters = lax.axis_size("heads")
    piece_rows = BLOCK // quarters
    row_count, col_count = points.shape
    block_count = row_count // BLOCK
    half_blocks = HALF // BLOCK
    patch_count = row_count // PATCH
    group_count = FF_GROUPS
    blocks = points.reshape(block_count, BLOCK, col_count)
    pieces = lax.dynamic_slice_in_dim(blocks, my_quarter * piece_rows, piece_rows, axis=1)
    for layer_index in range(LAYERS):
        shifted = layer_index % 2 == 1
        up_full = lax.all_gather(w_up[layer_index], "heads", axis=1, tiled=True)
        down_full = lax.all_gather(w_down[layer_index], "heads", axis=0, tiled=True)
        grouped = regroup(pieces, perm[layer_index], my_shard)
        normed = layer_norm(grouped, ln_attn[layer_index])
        if shifted:
            head_tiles = from_behind(
                jnp.stack([grouped[:half_blocks], normed[:half_blocks]]), "pts", -1
            )
            grouped = jnp.concatenate([grouped[half_blocks:], head_tiles[0]], axis=0)
            normed = jnp.concatenate([normed[half_blocks:], head_tiles[1]], axis=0)
        full_normed = gather_rows(normed)
        live_counts = lax.dynamic_slice_in_dim(
            counts[layer_index], my_shard * patch_count, patch_count
        )
        queries = jnp.dot(full_normed, w_query[layer_index], preferred_element_type=jnp.float32)
        key_rows = jnp.dot(full_normed, w_key[layer_index], preferred_element_type=jnp.float32)
        values = jnp.dot(
            full_normed, w_value[layer_index], preferred_element_type=jnp.float32
        ).astype(jnp.bfloat16)
        local_heads = queries.shape[1] // HD

        def to_tiles(matrix):
            return matrix.reshape(patch_count, PATCH, local_heads, HD)

        heads_out = patch_attention(
            to_tiles(queries), to_tiles(key_rows), to_tiles(values), live_counts
        )
        heads_out = heads_out.reshape(block_count, quarters, piece_rows, local_heads * HD)
        my_heads_out = lax.all_to_all(heads_out, "heads", split_axis=1, concat_axis=3, tiled=True)
        my_heads_out = my_heads_out.reshape(block_count * piece_rows, quarters * local_heads * HD)
        my_rows = grouped.reshape(block_count * piece_rows, col_count)
        attn_mixed = jnp.dot(my_heads_out, w_proj[layer_index], preferred_element_type=jnp.float32)
        residual = (my_rows.astype(jnp.float32) + attn_mixed).astype(jnp.bfloat16)
        normed_mlp = layer_norm(residual, ln_mlp[layer_index])
        hidden = jax.nn.gelu(
            jnp.dot(normed_mlp, up_full, preferred_element_type=jnp.float32),
            approximate=False,
        ).astype(jnp.bfloat16)
        group_width = up_full.shape[1] // group_count
        hidden_groups = hidden.reshape(hidden.shape[0], group_count, group_width)
        down_groups = down_full.reshape(group_count, group_width, col_count)
        mlp_terms = jnp.einsum(
            "rgf,gfc->grc", hidden_groups, down_groups, preferred_element_type=jnp.float32
        ).astype(jnp.bfloat16)
        mlp_total = jnp.sum(mlp_terms.astype(jnp.float32), axis=0)
        stream = (residual.astype(jnp.float32) + mlp_total).astype(jnp.bfloat16)
        pieces = stream.reshape(block_count, piece_rows, col_count)
        if shifted:
            tail_tiles = from_behind(pieces[block_count - half_blocks :], "pts", 1)
            pieces = jnp.concatenate([tail_tiles, pieces[: block_count - half_blocks]], axis=0)
    return gather_rows(pieces)


def solution(mesh):
    placed = (
        P("pts", None),
        P(),
        P(),
        P(),
        P(None, None, "heads"),
        P(None, None, "heads"),
        P(None, None, "heads"),
        P(),
        P(),
        P(None, None, "heads"),
        P(None, "heads", None),
    )
    return jax.shard_map(
        shards, mesh=mesh, in_specs=placed, out_specs=P("pts", None), check_vma=False
    )
```
